256 devices in a mesh: section: 4 (over x), space: 64 (over z, y, core).
Axes of the slice: x: 4, y: 4, z: 8, core: 2. Of those that a mesh axis runs over, the one named last changes fastest.
Arguments:
- volumes: bfloat16 [4, 512, 16, 16, 128], P(None, 'space'), may hold values from -6 to 6
- kernels: bfloat16 [4, 3, 3, 3, 128, 128], P('section'), may hold values from -0.109375 to 0.109375
- scales: float32 [4, 128], P('section'), may hold values from 1 to 3
- shifts: float32 [4, 128], P('section'), may hold values from -0.5 to 0.5
Outputs:
- activations: bfloat16 [4, 4, 512, 16, 16, 128], P('section', None, 'space')
The draws below stay inside these ranges and needn't reach their ends.
All inputs are finite; a program needn't handle non-finite values.
Results may differ from the reference program's by a relative error of at most 0.006.
Values may be sent and summed in bfloat16 or wider, within the bound.
No kernel may reach another device: no remote copies, remote signals or barrier semaphores. Data moves between devices by JAX's collectives and lax.ppermute only.
A program may use at most 128 MiB of HBM per device.

```python
import math
import jax
import jax.numpy as jnp
from jax import lax

C = 128
Y = 16
Z = 16
MB = 4
SECTIONS = 4
X = 512


def steps_of(own_key, dims, pieces, low, top_value):
    factor_of, own = 1.0, jax.random.fold_in(own_key, 6)
    for position, blocks in pieces:
        steps = jnp.exp(jax.random.uniform(jax.random.fold_in(own, position), (blocks,), jnp.float32, low / len(pieces), top_value / len(pieces)))
        factor_of = factor_of * jnp.repeat(steps, dims[position] // blocks).reshape([-1 if axis == position else 1 for axis in range(len(dims))])
    return factor_of


def normal_values(stream_key, dims, width, most, cuts=(), kind=jnp.bfloat16):
    entries = width * jax.random.normal(stream_key, dims, jnp.float32)
    if cuts:
        entries = entries * steps_of(stream_key, dims, cuts, -0.22, 0.18)
    return jnp.clip(entries, -most, most).astype(kind)


def setup_inputs(seed: int = 0) -> dict:
    key_of = jax.random.split(jax.random.key(seed), 5)
    return {
        "volumes": normal_values(key_of[0], (MB, X, Y, Z, C), 1.0, 6.0, ((1, 64),)),
        "kernels": normal_values(key_of[1], (SECTIONS, 3, 3, 3, C, C), (27 * C) ** -0.5, 0.109375, ((0, 4),)),
        "scales": jnp.clip(jnp.exp(math.log(3.0) - 1.0986123 * jax.random.uniform(key_of[2], (SECTIONS, C), jnp.float32) ** steps_of(key_of[2], (SECTIONS, C), ((0, 4),), -0.2, 0.2)), 1.0, 3.0),
        "shifts": jnp.clip(jax.random.uniform(key_of[3], (SECTIONS, C), jnp.float32, -0.5, 0.5) * steps_of(key_of[3], (SECTIONS, C), ((0, 4),), -0.4, 0.0), -0.5, 0.5),
    }


def section_layer(field, kernel, scale, shift):
    conv = lax.conv_general_dilated(field.astype(jnp.float32)[None], kernel.astype(jnp.float32), (1, 1, 1), "SAME", dimension_numbers=("NDHWC", "DHWIO", "NDHWC"), precision=lax.Precision.HIGHEST)[0]
    return jnp.maximum(conv * scale + shift, 0.0).astype(jnp.bfloat16)


def reference(volumes, kernels, scales, shifts):
    per_section = []
    current = volumes
    for section_id in range(SECTIONS):
        outputs = []
        for batch_id in range(MB):
            outputs.append(section_layer(current[batch_id], kernels[section_id], scales[section_id], shifts[section_id]))
        current = jnp.stack(outputs)
        per_section.append(current)
    return jnp.stack(per_section)
```

```python
import jax
import jax.numpy as jnp
from jax import lax
from jax.sharding import PartitionSpec as P


def halos(value):
    size = lax.axis_size("space")
    up = [(i, i + 1) for i in range(size - 1)]
    down = [(i + 1, i) for i in range(size - 1)]
    before = lax.ppermute(value[-1:], "space", up)
    after = lax.ppermute(value[:1], "space", down)
    return before, after


def conv(field, kernel):
    return lax.conv_general_dilated(
        field[None],
        kernel,
        (1, 1, 1),
        ((0, 0), (1, 1), (1, 1)),
        dimension_numbers=("NDHWC", "DHWIO", "NDHWC"),
        preferred_element_type=jnp.float32,
    )[0]


def layer(field, kernel, scale, shift):
    before, after = halos(field)
    first = conv(jnp.concatenate([before, field[:2]]), kernel)
    inner = conv(field, kernel)
    last = conv(jnp.concatenate([field[-2:], after]), kernel)
    parts = [first, inner, last]
    return jnp.concatenate(
        [jnp.maximum(p * scale + shift, 0.0).astype(jnp.bfloat16) for p in parts]
    )


def gather_kernels(kernels):
    core = lax.axis_index("space") % 2
    chans = kernels.shape[-1]
    half = chans // 2
    mine = lax.dynamic_slice_in_dim(kernels[0], core * half, half, axis=-1)
    gathered = lax.all_gather(mine, "section")
    size = lax.axis_size("space")
    pairs = [(i, i ^ 1) for i in range(size)]
    other = lax.ppermute(gathered, "space", pairs)
    low = jnp.where(core == 0, gathered, other)
    high = jnp.where(core == 0, other, gathered)
    return jnp.concatenate([low, high], axis=-1)


def on_device(volumes, kernels, scales, shifts):
    me = lax.axis_index("section")
    sections = lax.axis_size("section")
    all_kernels = gather_kernels(kernels)
    all_scales = lax.all_gather(scales[0], "section")
    all_shifts = lax.all_gather(shifts[0], "section")
    field = lax.dynamic_index_in_dim(volumes, me, 0, keepdims=False)
    pieces = []
    for s in range(sections):
        field = layer(field, all_kernels[s], all_scales[s], all_shifts[s])
        row = [field]
        for d in range(1, sections):
            source = (s - d) % sections
            row.append(lax.ppermute(field, "section", [(source, s)]))
        pieces.append(row)
    count = volumes.shape[0]
    outs = []
    for m in range(count):
        pick = pieces[0][(0 - m) % sections]
        for s in range(1, sections):
            pick = jnp.where(me == s, pieces[s][(s - m) % sections], pick)
        outs.append(pick)
    return jnp.stack(outs)[None]


def solution(mesh):
    return jax.shard_map(
        on_device,
        mesh=mesh,
        in_specs=(
            P(None, "space", None, None, None),
            P("section", None, None, None, None, None),
            P("section", None),
            P("section", None),
        ),
        out_specs=P("section", None, "space", None, None, None),
        check_vma=False,
    )
```

```python
import jax
import jax.numpy as jnp
from jax import lax
from jax.sharding import PartitionSpec as P


def halos(value):
    size = lax.axis_size("space")
    up = [(i, i + 1) for i in range(size - 1)]
    down = [(i + 1, i) for i in range(size - 1)]
    before = lax.ppermute(value[-1:], "space", up)
    after = lax.ppermute(value[:1], "space", down)
    return before, after


def conv(field, kernel):
    return lax.conv_general_dilated(
        field[None],
        kernel,
        (1, 1, 1),
        ((0, 0), (1, 1), (1, 1)),
        dimension_numbers=("NDHWC", "DHWIO", "NDHWC"),
        preferred_element_type=jnp.float32,
    )[0]


def layer(field, kernel, scale, shift):
    before, after = halos(field)
    first = conv(jnp.concatenate([before, field[:2]]), kernel)
    inner = conv(field, kernel)
    last = conv(jnp.concatenate([field[-2:], after]), kernel)
    parts = [first, inner, last]
    return jnp.concatenate(
        [jnp.maximum(p * scale + shift, 0.0).astype(jnp.bfloat16) for p in parts]
    )


def shifted_copies(value, count):
    pairs_of = lambda d: [(i, (i + d) % count) for i in range(count)]
    return [lax.ppermute(value, "section", pairs_of(d)) for d in range(1, count)]


def gather_params(kernels, scales, shifts):
    me = lax.axis_index("section")
    count = lax.axis_size("section")
    core = lax.axis_index("space") % 2
    half = kernels.shape[-1] // 2
    mine = lax.dynamic_slice_in_dim(kernels[0], core * half, half, axis=-1)
    affine = jnp.concatenate([scales, shifts])
    halves = jnp.stack([mine] + shifted_copies(mine, count))
    affines = jnp.stack([affine] + shifted_copies(affine, count))
    size = lax.axis_size("space")
    other = lax.ppermute(halves, "space", [(i, i ^ 1) for i in range(size)])
    low = jnp.where(core == 0, halves, other)
    high = jnp.where(core == 0, other, halves)
    by_shift = jnp.concatenate([low, high], axis=-1)
    order = [(me - t) % count for t in range(count)]
    pick = lambda stack, t: lax.dynamic_index_in_dim(stack, order[t], 0, keepdims=False)
    return [(pick(by_shift, t), pick(affines, t)) for t in range(count)]


def on_device(volumes, kernels, scales, shifts):
    me = lax.axis_index("section")
    sections = lax.axis_size("section")
    params = gather_params(kernels, scales, shifts)
    field = lax.dynamic_index_in_dim(volumes, me, 0, keepdims=False)
    pieces = []
    for s in range(sections):
        if s >= 2:
            field, pieces[s - 2] = lax.optimization_barrier((field, pieces[s - 2]))
        kernel, affine = params[s]
        field = layer(field, kernel, affine[0], affine[1])
        row = [field]
        for d in range(1, sections):
            source = (s - d) % sections
            row.append(lax.ppermute(field, "section", [(source, s)]))
        pieces.append(row)
    count = volumes.shape[0]
    outs = []
    for m in range(count):
        pick = pieces[0][(0 - m) % sections]
        for s in range(1, sections):
            pick = jnp.where(me == s, pieces[s][(s - m) % sections], pick)
        outs.append(pick)
    return jnp.stack(outs)[None]


def solution(mesh):
    return jax.shard_map(
        on_device,
        mesh=mesh,
        in_specs=(
            P(None, "space", None, None, None),
            P("section", None, None, None, None, None),
            P("section", None),
            P("section", None),
        ),
        out_specs=P("section", None, "space", None, None, None),
        check_vma=False,
    )
```

```python
import jax
import jax.numpy as jnp
from jax import lax
from jax.sharding import PartitionSpec as P


def conv(field, kernel):
    return lax.conv_general_dilated(
        field[None],
        kernel,
        (1, 1, 1),
        ((0, 0), (1, 1), (1, 1)),
        dimension_numbers=("NDHWC", "DHWIO", "NDHWC"),
        preferred_element_type=jnp.float32,
    )[0]


def with_halo(block, depth):
    size = lax.axis_size("space")
    up = [(i, i + 1) for i in range(size - 1)]
    down = [(i + 1, i) for i in range(size - 1)]
    before = lax.ppermute(block[-depth:], "space", up)
    after = lax.ppermute(block[:depth], "space", down)
    return jnp.concatenate([before, block, after])


def shifted_copies(value, count):
    pairs_of = lambda d: [(i, (i + d) % count) for i in range(count)]
    return [lax.ppermute(value, "section", pairs_of(d)) for d in range(1, count)]


def gather_params(kernels, scales, shifts):
    me = lax.axis_index("section")
    count = lax.axis_size("section")
    core = lax.axis_index("space") % 2
    half = kernels.shape[-1] // 2
    mine = lax.dynamic_slice_in_dim(kernels[0], core * half, half, axis=-1)
    halves = jnp.stack([mine] + shifted_copies(mine, count))
    size = lax.axis_size("space")
    other = lax.ppermute(halves, "space", [(i, i ^ 1) for i in range(size)])
    low = jnp.where(core == 0, halves, other)
    high = jnp.where(core == 0, other, halves)
    by_shift = jnp.concatenate([low, high], axis=-1)
    affine = jnp.concatenate([scales, shifts])[None]
    slots = jnp.arange(count)[:, None, None] == me
    affines = lax.psum(jnp.where(slots, affine, 0.0), "section")
    kernel_of = lambda t: lax.dynamic_index_in_dim(by_shift, (me - t) % count, 0, keepdims=False)
    return [(kernel_of(t), affines[t]) for t in range(count)]


def on_device(volumes, kernels, scales, shifts):
    me = lax.axis_index("section")
    place = lax.axis_index("space")
    sections = lax.axis_size("section")
    places = lax.axis_size("space")
    depth = volumes.shape[1]
    params = gather_params(kernels, scales, shifts)
    block = lax.dynamic_index_in_dim(volumes, me, 0, keepdims=False)
    field = with_halo(block, sections)
    done = []
    for s in range(sections):
        kernel, affine = params[s]
        total = conv(field, kernel)
        field = jnp.maximum(total * affine[0] + affine[1], 0.0).astype(jnp.bfloat16)
        margin = sections - 1 - s
        if margin:
            plane = place * depth - margin + jnp.arange(field.shape[0])
            inside = (plane >= 0) & (plane < places * depth)
            field = jnp.where(inside[:, None, None, None], field, jnp.zeros_like(field))
            done.append(field[margin:-margin])
        else:
            done.append(field)
    stacked = jnp.stack(done)
    received = [stacked[me]]
    for d in range(1, sections):
        outgoing = lax.dynamic_index_in_dim(stacked, (me + d) % sections, 0, keepdims=False)
        pairs = [(i, (i + d) % sections) for i in range(sections)]
        received.append(lax.ppermute(outgoing, "section", pairs))
    by_lag = jnp.stack(received)
    count = volumes.shape[0]
    outs = [
        lax.dynamic_index_in_dim(by_lag, (me - m) % sections, 0, keepdims=False)
        for m in range(count)
    ]
    return jnp.stack(outs)[None]


def solution(mesh):
    return jax.shard_map(
        on_device,
        mesh=mesh,
        in_specs=(
            P(None, "space", None, None, None),
            P("section", None, None, None, None, None),
            P("section", None),
            P("section", None),
        ),
        out_specs=P("section", None, "space", None, None, None),
        check_vma=False,
    )
```

```python
import jax
import jax.numpy as jnp
from jax import lax
from jax.sharding import PartitionSpec as P


def conv(field, kernel):
    return lax.conv_general_dilated(
        field[None],
        kernel,
        (1, 1, 1),
        ((0, 0), (1, 1), (1, 1)),
        dimension_numbers=("NDHWC", "DHWIO", "NDHWC"),
        preferred_element_type=jnp.float32,
    )[0]


def with_halo(block, depth):
    size = lax.axis_size("space")
    up = [(i, i + 1) for i in range(size - 1)]
    down = [(i + 1, i) for i in range(size - 1)]
    before = lax.ppermute(block[-depth:], "space", up)
    after = lax.ppermute(block[:depth], "space", down)
    return jnp.concatenate([before, block, after])


def shifted_copies(value, count):
    pairs_of = lambda d: [(i, (i + d) % count) for i in range(count)]
    return [lax.ppermute(value, "section", pairs_of(d)) for d in range(1, count)]


def exact_pieces(value):
    pieces = []
    rest = value
    for _ in range(3):
        piece = rest.astype(jnp.bfloat16)
        pieces.append(piece)
        rest = rest - piece.astype(jnp.float32)
    return pieces


def gather_params(kernels, scales, shifts):
    me = lax.axis_index("section")
    count = lax.axis_size("section")
    core = lax.axis_index("space") % 2
    half = kernels.shape[-1] // 2
    taps = kernels.shape[1:-1]
    mine = lax.dynamic_slice_in_dim(kernels[0], core * half, half, axis=-1)
    rows = mine.reshape(-1, half)
    split = rows.shape[0]
    affine = lax.dynamic_slice_in_dim(jnp.concatenate([scales, shifts]), core * half, half, axis=-1)
    payload = jnp.concatenate([rows] + exact_pieces(affine))
    stack = jnp.stack([payload] + shifted_copies(payload, count))
    size = lax.axis_size("space")
    other = lax.ppermute(stack, "space", [(i, i ^ 1) for i in range(size)])
    low = jnp.where(core == 0, stack, other)
    high = jnp.where(core == 0, other, stack)
    by_shift = jnp.concatenate([low, high], axis=-1)
    params = []
    for t in range(count):
        entry = lax.dynamic_index_in_dim(by_shift, (me - t) % count, 0, keepdims=False)
        kernel = entry[:split].reshape(taps + (2 * half,))
        extra = entry[split:].astype(jnp.float32)
        scale = extra[0] + extra[2] + extra[4]
        shift = extra[1] + extra[3] + extra[5]
        params.append((kernel, (scale, shift)))
    return params


def on_device(volumes, kernels, scales, shifts):
    me = lax.axis_index("section")
    place = lax.axis_index("space")
    sections = lax.axis_size("section")
    places = lax.axis_size("space")
    depth = volumes.shape[1]
    block = lax.dynamic_index_in_dim(volumes, me, 0, keepdims=False)
    field = with_halo(block, sections)
    params = gather_params(kernels, scales, shifts)
    done = []
    early = []
    for s in range(sections):
        if s == sections - 1:
            stacked = jnp.stack(done)
            for d in range(1, sections):
                target = (me + d) % sections
                outgoing = lax.dynamic_index_in_dim(
                    stacked, jnp.minimum(target, sections - 2), 0, keepdims=False
                )
                pairs = [(i, (i + d) % sections) for i in range(sections)]
                pairs = [p for p in pairs if p[1] != sections - 1]
                early.append(lax.ppermute(outgoing, "section", pairs))
        kernel, affine = params[s]
        total = conv(field, kernel)
        field = jnp.maximum(total * affine[0] + affine[1], 0.0).astype(jnp.bfloat16)
        margin = sections - 1 - s
        if margin:
            plane = place * depth - margin + jnp.arange(field.shape[0])
            inside = (plane >= 0) & (plane < places * depth)
            field = jnp.where(inside[:, None, None, None], field, jnp.zeros_like(field))
            done.append(field[margin:-margin])
        else:
            done.append(field)
    last = sections - 1
    received = [jnp.stack(done)[me]]
    for d in range(1, sections):
        late = lax.ppermute(done[last], "section", [((last - d) % sections, last)])
        received.append(jnp.where(me == last, late, early[d - 1]))
    by_lag = jnp.stack(received)
    count = volumes.shape[0]
    outs = [
        lax.dynamic_index_in_dim(by_lag, (me - m) % sections, 0, keepdims=False)
        for m in range(count)
    ]
    return jnp.stack(outs)[None]


def solution(mesh):
    return jax.shard_map(
        on_device,
        mesh=mesh,
        in_specs=(
            P(None, "space", None, None, None),
            P("section", None, None, None, None, None),
            P("section", None),
            P("section", None),
        ),
        out_specs=P("section", None, "space", None, None, None),
        check_vma=False,
    )
```

```python
import jax
import jax.numpy as jnp
from jax import lax
from jax.sharding import PartitionSpec as P


def conv(field, kernel):
    return lax.conv_general_dilated(
        field[None],
        kernel,
        (1, 1, 1),
        ((0, 0), (1, 1), (1, 1)),
        dimension_numbers=("NDHWC", "DHWIO", "NDHWC"),
        preferred_element_type=jnp.float32,
    )[0]


def with_halo(block, depth):
    size = lax.axis_size("space")
    up = [(i, i + 1) for i in range(size - 1)]
    down = [(i + 1, i) for i in range(size - 1)]
    before = lax.ppermute(block[-depth:], "space", up)
    after = lax.ppermute(block[:depth], "space", down)
    return jnp.concatenate([before, block, after])


def shifted_copies(value, count):
    pairs_of = lambda d: [(i, (i + d) % count) for i in range(count)]
    return [lax.ppermute(value, "section", pairs_of(d)) for d in range(1, count)]


def gather_params(kernels, scales, shifts):
    me = lax.axis_index("section")
    count = lax.axis_size("section")
    core = lax.axis_index("space") % 2
    half = kernels.shape[-1] // 2
    mine = lax.dynamic_slice_in_dim(kernels[0], core * half, half, axis=-1)
    halves = jnp.stack([mine] + shifted_copies(mine, count))
    size = lax.axis_size("space")
    other = lax.ppermute(halves, "space", [(i, i ^ 1) for i in range(size)])
    low = jnp.where(core == 0, halves, other)
    high = jnp.where(core == 0, other, halves)
    by_shift = jnp.concatenate([low, high], axis=-1)
    affine = jnp.concatenate([scales, shifts])
    affines = jnp.stack([affine] + shifted_copies(affine, count))
    pick = lambda stack, t: lax.dynamic_index_in_dim(stack, (me - t) % count, 0, keepdims=False)
    return [(pick(by_shift, t), pick(affines, t)) for t in range(count)]


def on_device(volumes, kernels, scales, shifts):
    me = lax.axis_index("section")
    place = lax.axis_index("space")
    sections = lax.axis_size("section")
    places = lax.axis_size("space")
    depth = volumes.shape[1]
    block = lax.dynamic_index_in_dim(volumes, me, 0, keepdims=False)
    field = with_halo(block, sections)
    params = gather_params(kernels, scales, shifts)
    done = []
    for s in range(sections):
        kernel, affine = params[s]
        total = conv(field, kernel)
        field = jnp.maximum(total * affine[0] + affine[1], 0.0).astype(jnp.bfloat16)
        margin = sections - 1 - s
        if margin:
            plane = place * depth - margin + jnp.arange(field.shape[0])
            inside = (plane >= 0) & (plane < places * depth)
            field = jnp.where(inside[:, None, None, None], field, jnp.zeros_like(field))
            done.append(field[margin:-margin])
        else:
            done.append(field)
    stacked = jnp.stack(done)
    received = [stacked[me]]
    for d in range(1, sections):
        outgoing = lax.dynamic_index_in_dim(stacked, (me + d) % sections, 0, keepdims=False)
        pairs = [(i, (i + d) % sections) for i in range(sections)]
        received.append(lax.ppermute(outgoing, "section", pairs))
    by_lag = jnp.stack(received)
    count = volumes.shape[0]
    outs = [
        lax.dynamic_index_in_dim(by_lag, (me - m) % sections, 0, keepdims=False)
        for m in range(count)
    ]
    return jnp.stack(outs)[None]


def solution(mesh):
    return jax.shard_map(
        on_device,
        mesh=mesh,
        in_specs=(
            P(None, "space", None, None, None),
            P("section", None, None, None, None, None),
            P("section", None),
            P("section", None),
        ),
        out_specs=P("section", None, "space", None, None, None),
        check_vma=False,
    )
```

```python
import jax
import jax.numpy as jnp
from jax import lax
from jax.sharding import PartitionSpec as P


def conv(field, kernel):
    return lax.conv_general_dilated(
        field[None],
        kernel,
        (1, 1, 1),
        ((0, 0), (1, 1), (1, 1)),
        dimension_numbers=("NDHWC", "DHWIO", "NDHWC"),
        preferred_element_type=jnp.float32,
    )[0]


def with_halo(block, depth):
    size = lax.axis_size("space")
    up = [(i, i + 1) for i in range(size - 1)]
    down = [(i + 1, i) for i in range(size - 1)]
    before = lax.ppermute(block[-depth:], "space", up)
    after = lax.ppermute(block[:depth], "space", down)
    return jnp.concatenate([before, block, after])


def shifted_copies(value, count):
    pairs_of = lambda d: [(i, (i + d) % count) for i in range(count)]
    return [lax.ppermute(value, "section", pairs_of(d)) for d in range(1, count)]


def gather_params(kernels, scales, shifts):
    me = lax.axis_index("section")
    count = lax.axis_size("section")
    core = lax.axis_index("space") % 2
    half = kernels.shape[-1] // 2
    mine = lax.dynamic_slice_in_dim(kernels[0], core * half, half, axis=-1)
    affine = jnp.concatenate([scales, shifts])
    moved = shifted_copies((mine, affine), count)
    halves = jnp.stack([mine] + [k for k, _ in moved])
    affines = jnp.stack([affine] + [a for _, a in moved])
    size = lax.axis_size("space")
    other = lax.ppermute(halves, "space", [(i, i ^ 1) for i in range(size)])
    low = jnp.where(core == 0, halves, other)
    high = jnp.where(core == 0, other, halves)
    by_shift = jnp.concatenate([low, high], axis=-1)
    pick = lambda stack, t: lax.dynamic_index_in_dim(stack, (me - t) % count, 0, keepdims=False)
    return [(pick(by_shift, t), pick(affines, t)) for t in range(count)]


def on_device(volumes, kernels, scales, shifts):
    me = lax.axis_index("section")
    place = lax.axis_index("space")
    sections = lax.axis_size("section")
    places = lax.axis_size("space")
    depth = volumes.shape[1]
    block = lax.dynamic_index_in_dim(volumes, me, 0, keepdims=False)
    field = with_halo(block, sections)
    params = gather_params(kernels, scales, shifts)
    done = []
    for s in range(sections):
        kernel, affine = params[s]
        total = conv(field, kernel)
        field = jnp.maximum(total * affine[0] + affine[1], 0.0).astype(jnp.bfloat16)
        margin = sections - 1 - s
        if margin:
            plane = place * depth - margin + jnp.arange(field.shape[0])
            inside = (plane >= 0) & (plane < places * depth)
            field = jnp.where(inside[:, None, None, None], field, jnp.zeros_like(field))
            done.append(field[margin:-margin])
        else:
            done.append(field)
    stacked = jnp.stack(done)
    ring = lambda d: [(i, (i + d) % sections) for i in range(sections)]
    toward = lambda d: lax.dynamic_index_in_dim(stacked, (me + d) % sections, 0, keepdims=False)
    received = [stacked[me]]
    received.append(lax.ppermute(toward(1), "section", ring(1)))
    far = toward(2)
    split = far.shape[0] // 2
    ahead = lax.ppermute(lax.ppermute(far[:split], "section", ring(1)), "section", ring(1))
    behind = lax.ppermute(lax.ppermute(far[split:], "section", ring(-1)), "section", ring(-1))
    received.append(jnp.concatenate([ahead, behind]))
    received.append(lax.ppermute(toward(-1), "section", ring(-1)))
    by_lag = jnp.stack(received)
    count = volumes.shape[0]
    outs = [
        lax.dynamic_index_in_dim(by_lag, (me - m) % sections, 0, keepdims=False)
        for m in range(count)
    ]
    return jnp.stack(outs)[None]


def solution(mesh):
    return jax.shard_map(
        on_device,
        mesh=mesh,
        in_specs=(
            P(None, "space", None, None, None),
            P("section", None, None, None, None, None),
            P("section", None),
            P("section", None),
        ),
        out_specs=P("section", None, "space", None, None, None),
        check_vma=False,
    )
```

```python
import jax
import jax.numpy as jnp
from jax import lax
from jax.sharding import PartitionSpec as P


def conv(field, kernel):
    return lax.conv_general_dilated(
        field[None],
        kernel,
        (1, 1, 1),
        ((0, 0), (1, 1), (1, 1)),
        dimension_numbers=("NDHWC", "DHWIO", "NDHWC"),
        preferred_element_type=jnp.float32,
    )[0]


def with_halo(block, depth):
    size = lax.axis_size("space")
    up = [(i, i + 1) for i in range(size - 1)]
    down = [(i + 1, i) for i in range(size - 1)]
    before = lax.ppermute(block[-depth:], "space", up)
    after = lax.ppermute(block[:depth], "space", down)
    return jnp.concatenate([before, block, after])


def shifted_copies(value, count):
    pairs_of = lambda d: [(i, (i + d) % count) for i in range(count)]
    return [lax.ppermute(value, "section", pairs_of(d)) for d in range(1, count)]


def exact_pieces(value):
    pieces = []
    rest = value
    for _ in range(3):
        piece = lax.reduce_precision(rest, exponent_bits=8, mantissa_bits=7)
        pieces.append(piece.astype(jnp.bfloat16))
        rest = rest - piece
    return pieces


def gather_params(kernels, scales, shifts, field):
    me = lax.axis_index("section")
    count = lax.axis_size("section")
    core = lax.axis_index("space") % 2
    half = kernels.shape[-1] // 2
    taps = kernels.shape[1:-2]
    mine = lax.dynamic_slice_in_dim(kernels[0], core * half, half, axis=-1)
    slabs = mine.reshape((-1,) + mine.shape[-2:])
    affine = lax.dynamic_slice_in_dim(jnp.concatenate([scales, shifts]), core * half, half, axis=-1)
    extra = jnp.concatenate(exact_pieces(affine))
    extra = jnp.pad(extra, ((0, slabs.shape[1] - extra.shape[0]), (0, 0)))
    payload = jnp.concatenate([slabs, extra[None]])
    moved = shifted_copies(payload, count)
    field, moved = lax.optimization_barrier((field, moved))
    stack = jnp.stack([payload] + moved)
    size = lax.axis_size("space")
    other = lax.ppermute(stack, "space", [(i, i ^ 1) for i in range(size)])
    low = jnp.where(core == 0, stack, other)
    high = jnp.where(core == 0, other, stack)
    by_shift = jnp.concatenate([low, high], axis=-1)
    taps_count = slabs.shape[0]
    params = []
    for t in range(count):
        entry = lax.dynamic_index_in_dim(by_shift, (me - t) % count, 0, keepdims=False)
        kernel = entry[:taps_count].reshape(taps + entry.shape[-2:-1] + (2 * half,))
        tail = entry[taps_count, :6].astype(jnp.float32)
        scale = tail[0] + tail[2] + tail[4]
        shift = tail[1] + tail[3] + tail[5]
        params.append((kernel, (scale, shift)))
    return field, params


def on_device(volumes, kernels, scales, shifts):
    me = lax.axis_index("section")
    place = lax.axis_index("space")
    sections = lax.axis_size("section")
    places = lax.axis_size("space")
    depth = volumes.shape[1]
    block = lax.dynamic_index_in_dim(volumes, me, 0, keepdims=False)
    field = with_halo(block, sections)
    field, params = gather_params(kernels, scales, shifts, field)
    done = []
    for s in range(sections):
        kernel, affine = params[s]
        total = conv(field, kernel)
        field = jnp.maximum(total * affine[0] + affine[1], 0.0).astype(jnp.bfloat16)
        margin = sections - 1 - s
        if margin:
            plane = place * depth - margin + jnp.arange(field.shape[0])
            inside = (plane >= 0) & (plane < places * depth)
            field = jnp.where(inside[:, None, None, None], field, jnp.zeros_like(field))
            done.append(field[margin:-margin])
        else:
            done.append(field)
    stacked = jnp.stack(done)
    received = [stacked[me]]
    for d in range(1, sections):
        outgoing = lax.dynamic_index_in_dim(stacked, (me + d) % sections, 0, keepdims=False)
        pairs = [(i, (i + d) % sections) for i in range(sections)]
        received.append(lax.ppermute(outgoing, "section", pairs))
    by_lag = jnp.stack(received)
    count = volumes.shape[0]
    outs = [
        lax.dynamic_index_in_dim(by_lag, (me - m) % sections, 0, keepdims=False)
        for m in range(count)
    ]
    return jnp.stack(outs)[None]


def solution(mesh):
    return jax.shard_map(
        on_device,
        mesh=mesh,
        in_specs=(
            P(None, "space", None, None, None),
            P("section", None, None, None, None, None),
            P("section", None),
            P("section", None),
        ),
        out_specs=P("section", None, "space", None, None, None),
        check_vma=False,
    )
```

```python
import jax
import jax.numpy as jnp
from jax import lax
from jax.sharding import PartitionSpec as P


def conv(field, kernel):
    return lax.conv_general_dilated(
        field[None],
        kernel,
        (1, 1, 1),
        ((0, 0), (1, 1), (1, 1)),
        dimension_numbers=("NDHWC", "DHWIO", "NDHWC"),
        preferred_element_type=jnp.float32,
    )[0]


def with_halo(block, depth):
    size = lax.axis_size("space")
    up = [(i, i + 1) for i in range(size - 1)]
    down = [(i + 1, i) for i in range(size - 1)]
    before = lax.ppermute(block[-depth:], "space", up)
    after = lax.ppermute(block[:depth], "space", down)
    return jnp.concatenate([before, block, after])


def shifted_copies(value, count):
    pairs_of = lambda d: [(i, (i + d) % count) for i in range(count)]
    return [lax.ppermute(value, "section", pairs_of(d)) for d in range(1, count)]


def gather_params(kernels, scales, shifts, field):
    me = lax.axis_index("section")
    count = lax.axis_size("section")
    core = lax.axis_index("space") % 2
    half = kernels.shape[-1] // 2
    mine = lax.dynamic_slice_in_dim(kernels[0], core * half, half, axis=-1)
    affine = jnp.concatenate([scales, shifts])
    moved = shifted_copies(mine, count)
    moved_affine = shifted_copies(affine, count)
    field, moved, moved_affine = lax.optimization_barrier((field, moved, moved_affine))
    halves = jnp.stack([mine] + moved)
    size = lax.axis_size("space")
    other = lax.ppermute(halves, "space", [(i, i ^ 1) for i in range(size)])
    low = jnp.where(core == 0, halves, other)
    high = jnp.where(core == 0, other, halves)
    by_shift = jnp.concatenate([low, high], axis=-1)
    affines = jnp.stack([affine] + moved_affine)
    pick = lambda stack, t: lax.dynamic_index_in_dim(stack, (me - t) % count, 0, keepdims=False)
    return field, [(pick(by_shift, t), pick(affines, t)) for t in range(count)]


def on_device(volumes, kernels, scales, shifts):
    me = lax.axis_index("section")
    place = lax.axis_index("space")
    sections = lax.axis_size("section")
    places = lax.axis_size("space")
    depth = volumes.shape[1]
    block = lax.dynamic_index_in_dim(volumes, me, 0, keepdims=False)
    field = with_halo(block, sections)
    field, params = gather_params(kernels, scales, shifts, field)
    done = []
    for s in range(sections):
        kernel, affine = params[s]
        total = conv(field, kernel)
        field = jnp.maximum(total * affine[0] + affine[1], 0.0).astype(jnp.bfloat16)
        margin = sections - 1 - s
        if margin:
            plane = place * depth - margin + jnp.arange(field.shape[0])
            inside = (plane >= 0) & (plane < places * depth)
            field = jnp.where(inside[:, None, None, None], field, jnp.zeros_like(field))
            done.append(field[margin:-margin])
        else:
            done.append(field)
    stacked = jnp.stack(done)
    received = [stacked[me]]
    for d in range(1, sections):
        outgoing = lax.dynamic_index_in_dim(stacked, (me + d) % sections, 0, keepdims=False)
        pairs = [(i, (i + d) % sections) for i in range(sections)]
        received.append(lax.ppermute(outgoing, "section", pairs))
    by_lag = jnp.stack(received)
    count = volumes.shape[0]
    outs = [
        lax.dynamic_index_in_dim(by_lag, (me - m) % sections, 0, keepdims=False)
        for m in range(count)
    ]
    return jnp.stack(outs)[None]


def solution(mesh):
    return jax.shard_map(
        on_device,
        mesh=mesh,
        in_specs=(
            P(None, "space", None, None, None),
            P("section", None, None, None, None, None),
            P("section", None),
            P("section", None),
        ),
        out_specs=P("section", None, "space", None, None, None),
        check_vma=False,
    )
```

```python
import jax
import jax.numpy as jnp
from jax import lax
from jax.sharding import PartitionSpec as P


def conv(field, kernel):
    return lax.conv_general_dilated(
        field[None],
        kernel,
        (1, 1, 1),
        ((0, 0), (1, 1), (1, 1)),
        dimension_numbers=("NDHWC", "DHWIO", "NDHWC"),
        preferred_element_type=jnp.float32,
    )[0]


def with_halo(block, depth):
    size = lax.axis_size("space")
    up = [(i, i + 1) for i in range(size - 1)]
    down = [(i + 1, i) for i in range(size - 1)]
    before = lax.ppermute(block[-depth:], "space", up)
    after = lax.ppermute(block[:depth], "space", down)
    return jnp.concatenate([before, block, after])


def shifted_copies(value, count):
    pairs_of = lambda d: [(i, (i + d) % count) for i in range(count)]
    return [lax.ppermute(value, "section", pairs_of(d)) for d in range(1, count)]


def gather_params(kernels, scales, shifts, field):
    me = lax.axis_index("section")
    count = lax.axis_size("section")
    core = lax.axis_index("space") % 2
    half = kernels.shape[-1] // 2
    mine = lax.dynamic_slice_in_dim(kernels[0], core * half, half, axis=-1)
    affine = jnp.concatenate([scales, shifts])
    moved = shifted_copies(mine, count)
    moved_affine = shifted_copies(affine, count)
    field, moved, moved_affine = lax.optimization_barrier((field, moved, moved_affine))
    halves = jnp.stack([mine] + moved)
    size = lax.axis_size("space")
    other = lax.ppermute(halves, "space", [(i, i ^ 1) for i in range(size)])
    low = jnp.where(core == 0, halves, other)
    high = jnp.where(core == 0, other, halves)
    by_shift = jnp.concatenate([low, high], axis=-1)
    affines = jnp.stack([affine] + moved_affine)
    pick = lambda stack, t: lax.dynamic_index_in_dim(stack, (me - t) % count, 0, keepdims=False)
    return field, [(pick(by_shift, t), pick(affines, t)) for t in range(count)]


def on_device(volumes, kernels, scales, shifts):
    me = lax.axis_index("section")
    place = lax.axis_index("space")
    sections = lax.axis_size("section")
    places = lax.axis_size("space")
    depth = volumes.shape[1]
    block = lax.dynamic_index_in_dim(volumes, me, 0, keepdims=False)
    field = with_halo(block, sections)
    field, params = gather_params(kernels, scales, shifts, field)
    done = []
    for s in range(sections):
        kernel, affine = params[s]
        total = conv(field, kernel)
        field = jnp.maximum(total * affine[0] + affine[1], 0.0).astype(jnp.bfloat16)
        margin = sections - 1 - s
        if margin:
            plane = place * depth - margin + jnp.arange(field.shape[0])
            inside = (plane >= 0) & (plane < places * depth)
            field = jnp.where(inside[:, None, None, None], field, jnp.zeros_like(field))
            done.append(field[margin:-margin])
        else:
            done.append(field)
    stacked = jnp.stack(done)
    return lax.all_to_all(stacked, "section", 0, 0, tiled=True)[None]


def solution(mesh):
    return jax.shard_map(
        on_device,
        mesh=mesh,
        in_specs=(
            P(None, "space", None, None, None),
            P("section", None, None, None, None, None),
            P("section", None),
            P("section", None),
        ),
        out_specs=P("section", None, "space", None, None, None),
        check_vma=False,
    )
```

```python
import jax
import jax.numpy as jnp
from jax import lax
from jax.sharding import PartitionSpec as P


def conv(field, kernel):
    return lax.conv_general_dilated(
        field[None],
        kernel,
        (1, 1, 1),
        ((0, 0), (1, 1), (1, 1)),
        dimension_numbers=("NDHWC", "DHWIO", "NDHWC"),
        preferred_element_type=jnp.float32,
    )[0]


def with_halo(block, depth):
    size = lax.axis_size("space")
    up = [(i, i + 1) for i in range(size - 1)]
    down = [(i + 1, i) for i in range(size - 1)]
    before = lax.ppermute(block[-depth:], "space", up)
    after = lax.ppermute(block[:depth], "space", down)
    return jnp.concatenate([before, block, after])


def shift(value, d, count):
    return lax.ppermute(value, "section", [(i, (i + d) % count) for i in range(count)])


def full_width(stack):
    core = lax.axis_index("space") % 2
    size = lax.axis_size("space")
    other = lax.ppermute(stack, "space", [(i, i ^ 1) for i in range(size)])
    low = jnp.where(core == 0, stack, other)
    high = jnp.where(core == 0, other, stack)
    return jnp.concatenate([low, high], axis=-1)


def gather_params(kernels, scales, shifts, field):
    count = lax.axis_size("section")
    core = lax.axis_index("space") % 2
    half = kernels.shape[-1] // 2
    mine = lax.dynamic_slice_in_dim(kernels[0], core * half, half, axis=-1)
    affine = jnp.concatenate([scales, shifts])
    near = [(shift(mine, d, count), shift(affine, d, count)) for d in (1, count - 1)]
    near, mine, affine = lax.optimization_barrier((near, mine, affine))
    far = (shift(mine, 2, count), shift(affine, 2, count))
    odd = (full_width(jnp.stack([near[0][0], near[1][0]])), jnp.stack([near[0][1], near[1][1]]))
    return odd, far


def on_device(volumes, kernels, scales, shifts):
    me = lax.axis_index("section")
    place = lax.axis_index("space")
    sections = lax.axis_size("section")
    places = lax.axis_size("space")
    depth = volumes.shape[1]
    block = lax.dynamic_index_in_dim(volumes, me, 0, keepdims=False)
    field = with_halo(block, sections)
    odd, far = gather_params(kernels, scales, shifts, field)
    own_affine = jnp.concatenate([scales, shifts])
    even = None
    steps = 2 * sections - 1
    arrived = []
    for t in range(steps):
        stage = t - me
        slot = ((2 * me - t) % sections) // 2
        if t == 0:
            kernel, affine = kernels[0], own_affine
        else:
            kernels_t, affines_t = odd if t % 2 else even
            kernel = lax.dynamic_index_in_dim(kernels_t, slot, 0, keepdims=False)
            affine = lax.dynamic_index_in_dim(affines_t, slot, 0, keepdims=False)
        total = conv(field, kernel)
        out = jnp.maximum(total * affine[0] + affine[1], 0.0).astype(jnp.bfloat16)
        margin = (out.shape[0] - depth) // 2
        plane = place * depth - margin + jnp.arange(out.shape[0])
        inside = (plane >= 0) & (plane < places * depth)
        out = jnp.where(inside[:, None, None, None], out, jnp.zeros_like(out))
        piece = out[margin : margin + depth]
        pairs = [(m, t - m) for m in range(sections) if 0 <= t - m < sections and t - m != m]
        if pairs:
            got = lax.ppermute(piece, "section", pairs)
        else:
            got = jnp.zeros_like(piece)
        arrived.append(jnp.where(t == 2 * me, piece, got))
        if t == 1:
            far, out = lax.optimization_barrier((far, out))
            far_full = full_width(far[0][None])[0]
            even = (jnp.stack([kernels[0], far_full]), jnp.stack([own_affine, far[1]]))
        if t < sections - 1:
            grown = jnp.pad(out, ((1, 1), (0, 0), (0, 0), (0, 0)))
            field = jnp.where(stage < 0, field, grown)
        else:
            field = out
    stacked = jnp.stack(arrived)
    count = volumes.shape[0]
    return lax.dynamic_slice_in_dim(stacked, me, count, axis=0)[None]


def solution(mesh):
    return jax.shard_map(
        on_device,
        mesh=mesh,
        in_specs=(
            P(None, "space", None, None, None),
            P("section", None, None, None, None, None),
            P("section", None),
            P("section", None),
        ),
        out_specs=P("section", None, "space", None, None, None),
        check_vma=False,
    )
```

```python
import jax
import jax.numpy as jnp
from jax import lax
from jax.sharding import PartitionSpec as P


def conv(field, kernel):
    return lax.conv_general_dilated(
        field[None],
        kernel,
        (1, 1, 1),
        ((0, 0), (1, 1), (1, 1)),
        dimension_numbers=("NDHWC", "DHWIO", "NDHWC"),
        preferred_element_type=jnp.float32,
    )[0]


def with_halo(block, depth):
    size = lax.axis_size("space")
    up = [(i, i + 1) for i in range(size - 1)]
    down = [(i + 1, i) for i in range(size - 1)]
    before = lax.ppermute(block[-depth:], "space", up)
    after = lax.ppermute(block[:depth], "space", down)
    return jnp.concatenate([before, block, after])


def shifted_copies(value, count):
    pairs_of = lambda d: [(i, (i + d) % count) for i in range(count)]
    return [lax.ppermute(value, "section", pairs_of(d)) for d in range(1, count)]


def gather_params(kernels, scales, shifts, field):
    me = lax.axis_index("section")
    count = lax.axis_size("section")
    core = lax.axis_index("space") % 2
    half = kernels.shape[-1] // 2
    mine = lax.dynamic_slice_in_dim(kernels[0], core * half, half, axis=-1)
    affine = jnp.concatenate([scales, shifts])
    moved = [lax.ppermute(mine, "section", [(i, (i + d) % count) for i in range(count)]) for d in (1, 3)]
    moved = [moved[0], None, moved[1]]
    moved_affine = shifted_copies(affine, count)
    field, moved, moved_affine = lax.optimization_barrier((field, moved, moved_affine))
    quarter = half // 2
    ring = lambda d: [(i, (i + d) % count) for i in range(count)]
    hop = lambda value, d: lax.ppermute(value, "section", ring(d))
    ahead = hop(hop(mine[..., :quarter], 1), 1)
    behind = hop(hop(mine[..., quarter:], -1), -1)
    moved[1] = jnp.concatenate([ahead, behind], axis=-1)
    halves = jnp.stack([mine] + moved)
    size = lax.axis_size("space")
    other = lax.ppermute(halves, "space", [(i, i ^ 1) for i in range(size)])
    low = jnp.where(core == 0, halves, other)
    high = jnp.where(core == 0, other, halves)
    by_shift = jnp.concatenate([low, high], axis=-1)
    affines = jnp.stack([affine] + moved_affine)
    pick = lambda stack, t: lax.dynamic_index_in_dim(stack, (me - t) % count, 0, keepdims=False)
    return field, [(pick(by_shift, t), pick(affines, t)) for t in range(count)]


def on_device(volumes, kernels, scales, shifts):
    me = lax.axis_index("section")
    place = lax.axis_index("space")
    sections = lax.axis_size("section")
    places = lax.axis_size("space")
    depth = volumes.shape[1]
    block = lax.dynamic_index_in_dim(volumes, me, 0, keepdims=False)
    field = with_halo(block, sections)
    field, params = gather_params(kernels, scales, shifts, field)
    done = []
    for s in range(sections):
        kernel, affine = params[s]
        total = conv(field, kernel)
        field = jnp.maximum(total * affine[0] + affine[1], 0.0).astype(jnp.bfloat16)
        margin = sections - 1 - s
        if margin:
            plane = place * depth - margin + jnp.arange(field.shape[0])
            inside = (plane >= 0) & (plane < places * depth)
            field = jnp.where(inside[:, None, None, None], field, jnp.zeros_like(field))
            done.append(field[margin:-margin])
        else:
            done.append(field)
    stacked = jnp.stack(done)
    return lax.all_to_all(stacked, "section", 0, 0, tiled=True)[None]


def solution(mesh):
    return jax.shard_map(
        on_device,
        mesh=mesh,
        in_specs=(
            P(None, "space", None, None, None),
            P("section", None, None, None, None, None),
            P("section", None),
            P("section", None),
        ),
        out_specs=P("section", None, "space", None, None, None),
        check_vma=False,
    )
```

```python
import jax
import jax.numpy as jnp
from jax import lax
from jax.sharding import PartitionSpec as P


def conv(field, kernel):
    return lax.conv_general_dilated(
        field[None],
        kernel,
        (1, 1, 1),
        ((0, 0), (1, 1), (1, 1)),
        dimension_numbers=("NDHWC", "DHWIO", "NDHWC"),
        preferred_element_type=jnp.float32,
    )[0]


def with_halo(block, depth):
    size = lax.axis_size("space")
    up = [(i, i + 1) for i in range(size - 1)]
    down = [(i + 1, i) for i in range(size - 1)]
    before = lax.ppermute(block[-depth:], "space", up)
    after = lax.ppermute(block[:depth], "space", down)
    return jnp.concatenate([before, block, after])


def shifted_copies(value, count):
    pairs_of = lambda d: [(i, (i + d) % count) for i in range(count)]
    return [lax.ppermute(value, "section", pairs_of(d)) for d in range(1, count)]


def gather_params(kernels, scales, shifts, field):
    me = lax.axis_index("section")
    count = lax.axis_size("section")
    core = lax.axis_index("space") % 2
    half = kernels.shape[-1] // 2
    mine = lax.dynamic_slice_in_dim(kernels[0], core * half, half, axis=-1)
    affine = jnp.concatenate([scales, shifts])
    moved = [lax.ppermute(mine, "section", [(i, (i + d) % count) for i in range(count)]) for d in (1, 3)]
    moved = [moved[0], None, moved[1]]
    moved_affine = shifted_copies(affine, count)
    field, moved, moved_affine = lax.optimization_barrier((field, moved, moved_affine))
    quarter = half // 2
    ring = lambda d: [(i, (i + d) % count) for i in range(count)]
    hop = lambda value, d: lax.ppermute(value, "section", ring(d))
    ahead = hop(hop(mine[..., :quarter], 1), 1)
    behind = hop(hop(mine[..., quarter:], -1), -1)
    moved[1] = jnp.concatenate([ahead, behind], axis=-1)
    halves = jnp.stack([mine] + moved)
    size = lax.axis_size("space")
    other = lax.ppermute(halves, "space", [(i, i ^ 1) for i in range(size)])
    low = jnp.where(core == 0, halves, other)
    high = jnp.where(core == 0, other, halves)
    by_shift = jnp.concatenate([low, high], axis=-1)
    affines = jnp.stack([affine] + moved_affine)
    pick = lambda stack, t: lax.dynamic_index_in_dim(stack, (me - t) % count, 0, keepdims=False)
    return field, [(pick(by_shift, t), pick(affines, t)) for t in range(count)]


def on_device(volumes, kernels, scales, shifts):
    me = lax.axis_index("section")
    place = lax.axis_index("space")
    sections = lax.axis_size("section")
    places = lax.axis_size("space")
    depth = volumes.shape[1]
    block = lax.dynamic_index_in_dim(volumes, me, 0, keepdims=False)
    field = with_halo(block, sections)
    field, params = gather_params(kernels, scales, shifts, field)
    done = []
    sent = []
    for s in range(sections):
        kernel, affine = params[s]
        total = conv(field, kernel)
        field = jnp.maximum(total * affine[0] + affine[1], 0.0).astype(jnp.bfloat16)
        margin = sections - 1 - s
        if margin:
            plane = place * depth - margin + jnp.arange(field.shape[0])
            inside = (plane >= 0) & (plane < places * depth)
            field = jnp.where(inside[:, None, None, None], field, jnp.zeros_like(field))
            done.append(field[margin:-margin])
        else:
            done.append(field)
        if s % 2 == 1:
            a, b = s - 1, s
            groups = [
                [(b, a), (a, b)],
                [(b + 1, a), (b + 2, b)],
                [(b + 2, a), (b + 1, b)],
            ]
            for pairs in groups:
                pairs = [(i % sections, j % sections) for i, j in pairs]
                to_b = [i for i, j in pairs if j == b][0]
                payload = jnp.where(me == to_b, done[b], done[a])
                sent.append(lax.ppermute(payload, "section", pairs))
    own = lax.dynamic_index_in_dim(jnp.stack(done), me, 0, keepdims=False)
    table = jnp.array([[6, 0, 1, 2], [0, 6, 2, 1], [4, 5, 6, 3], [5, 4, 3, 6]], jnp.int32)
    pool = jnp.stack(sent + [own])
    picks = table[me]
    count = volumes.shape[0]
    outs = [lax.dynamic_index_in_dim(pool, picks[m], 0, keepdims=False) for m in range(count)]
    return jnp.stack(outs)[None]


def solution(mesh):
    return jax.shard_map(
        on_device,
        mesh=mesh,
        in_specs=(
            P(None, "space", None, None, None),
            P("section", None, None, None, None, None),
            P("section", None),
            P("section", None),
        ),
        out_specs=P("section", None, "space", None, None, None),
        check_vma=False,
    )
```

```python
import jax
import jax.numpy as jnp
from jax import lax
from jax.sharding import PartitionSpec as P


def conv(field, kernel):
    return lax.conv_general_dilated(
        field[None],
        kernel,
        (1, 1, 1),
        ((0, 0), (1, 1), (1, 1)),
        dimension_numbers=("NDHWC", "DHWIO", "NDHWC"),
        preferred_element_type=jnp.float32,
    )[0]


def with_halo(block, depth):
    size = lax.axis_size("space")
    up = [(i, i + 1) for i in range(size - 1)]
    down = [(i + 1, i) for i in range(size - 1)]
    before = lax.ppermute(block[-depth:], "space", up)
    after = lax.ppermute(block[:depth], "space", down)
    return jnp.concatenate([before, block, after])


def shifted_copies(value, count):
    pairs_of = lambda d: [(i, (i + d) % count) for i in range(count)]
    return [lax.ppermute(value, "section", pairs_of(d)) for d in range(1, count)]


def gather_params(kernels, scales, shifts, field):
    me = lax.axis_index("section")
    count = lax.axis_size("section")
    core = lax.axis_index("space") % 2
    half = kernels.shape[-1] // 2
    mine = lax.dynamic_slice_in_dim(kernels[0], core * half, half, axis=-1)
    affine = jnp.concatenate([scales, shifts])
    quarter = half // 2
    ring = lambda d: [(i, (i + d) % count) for i in range(count)]
    hop = lambda value, d: lax.ppermute(value, "section", ring(d))
    first = [hop(mine[..., :quarter], 1), hop(mine[..., quarter:], -1)]
    moved_affine = shifted_copies(affine, count)
    field, first, moved_affine, sent = lax.optimization_barrier((field, first, moved_affine, mine))
    far = jnp.concatenate([hop(first[0], 1), hop(first[1], -1)], axis=-1)
    moved = [hop(sent, 1), far, hop(sent, count - 1)]
    halves = jnp.stack([mine] + moved)
    size = lax.axis_size("space")
    other = lax.ppermute(halves, "space", [(i, i ^ 1) for i in range(size)])
    low = jnp.where(core == 0, halves, other)
    high = jnp.where(core == 0, other, halves)
    by_shift = jnp.concatenate([low, high], axis=-1)
    affines = jnp.stack([affine] + moved_affine)
    pick = lambda stack, t: lax.dynamic_index_in_dim(stack, (me - t) % count, 0, keepdims=False)
    return field, [(pick(by_shift, t), pick(affines, t)) for t in range(count)]


def on_device(volumes, kernels, scales, shifts):
    me = lax.axis_index("section")
    place = lax.axis_index("space")
    sections = lax.axis_size("section")
    places = lax.axis_size("space")
    depth = volumes.shape[1]
    block = lax.dynamic_index_in_dim(volumes, me, 0, keepdims=False)
    field = with_halo(block, sections)
    field, params = gather_params(kernels, scales, shifts, field)
    done = []
    for s in range(sections):
        kernel, affine = params[s]
        total = conv(field, kernel)
        field = jnp.maximum(total * affine[0] + affine[1], 0.0).astype(jnp.bfloat16)
        margin = sections - 1 - s
        if margin:
            plane = place * depth - margin + jnp.arange(field.shape[0])
            inside = (plane >= 0) & (plane < places * depth)
            field = jnp.where(inside[:, None, None, None], field, jnp.zeros_like(field))
            done.append(field[margin:-margin])
        else:
            done.append(field)
    stacked = jnp.stack(done)
    return lax.all_to_all(stacked, "section", 0, 0, tiled=True)[None]


def solution(mesh):
    return jax.shard_map(
        on_device,
        mesh=mesh,
        in_specs=(
            P(None, "space", None, None, None),
            P("section", None, None, None, None, None),
            P("section", None),
            P("section", None),
        ),
        out_specs=P("section", None, "space", None, None, None),
        check_vma=False,
    )
```
